32 devices in a mesh: lat: 16 (over z, y, core), tm: 2 (over x).
Axes of the slice: x: 2, y: 2, z: 4, core: 2. Of those that a mesh axis runs over, the one named last changes fastest.
Arguments:
- fields: bfloat16 [3, 20, 640, 16, 64], P(None, None, 'lat', None, 'tm'), may hold values from -6 to 6
- vmodes: bfloat16 [20, 16], replicated, may hold values from -1.25 to 1.25
- owner_map: int32 [16], replicated, may hold values from 0 to 15, each once
- hough_table: bfloat16 [16, 15360, 1920], P('tm', 'lat'), may hold values from -0.125 to 0.125
- keep_mask: int32 [16, 15360], P('tm', 'lat'), may hold values 0 or 1
Outputs:
- filtered_fields: bfloat16 [16, 3, 640, 16, 64], P(None, None, 'lat', None, 'tm')
The draws below stay inside these ranges and needn't reach their ends.
Inputs may be any that keep to these rules, and one draw needn't show every extreme that they name: owner_map is a permutation of 0 to 15; order m uses the rows of hough_table and keep_mask of owner slot owner_map[m].
All inputs are finite; a program needn't handle non-finite values. No bound on the sum of `keep_mask` on one device may be relied on, other than what follows from the above.
Results may differ from the reference program's by a relative error of at most 0.0055.
Values may be sent and summed in bfloat16 or wider, within the bound.
No kernel may reach another device: no remote copies, remote signals or barrier semaphores. Data moves between devices by JAX's collectives and lax.ppermute only.
A program may use at most 128 MiB of HBM per device.

```python
import jax
import jax.numpy as jnp
from jax import lax

ORDERS = 16
KMODES = 16
HOUGH = 960
LATS = 640
LEV = 20
TIMES = 32


def place_ends(result, stream_key, smallest, high):
    longest = result.shape.index(max(result.shape))
    spots = []
    for shift in (0, 1):
        where = [jax.random.randint(jax.random.fold_in(stream_key, axis), (), 0, length) for axis, length in enumerate(result.shape)]
        where[longest] = (where[longest] + shift) % result.shape[longest]
        spots.append(tuple(where))
    return result.at[spots[0]].set(smallest).at[spots[1]].set(high)


def levels(key, shape, split, least, high):
    factor_of, own = 1.0, jax.random.fold_in(key, 6)
    for position, blocks in split:
        steps = jnp.exp(jax.random.uniform(jax.random.fold_in(own, position), (blocks,), jnp.float32, least / len(split), high / len(split)))
        factor_of = factor_of * jnp.repeat(steps, shape[position] // blocks).reshape([-1 if axis == position else 1 for axis in range(len(shape))])
    return factor_of


def normal_values(rng, extent, spread, limit, shards=(), held_as=jnp.bfloat16):
    level = levels(rng, extent, shards, -0.22, 0.18) if shards else 1.0
    result = jax.random.normal(rng, extent, jnp.float32) * spread * level
    return jnp.minimum(jnp.maximum(result, -limit), limit).astype(held_as)


def setup_inputs(seed: int = 0) -> dict:
    seeds = jax.random.split(jax.random.key(seed), 6)
    return {
        "fields": normal_values(seeds[0], (3, LEV, LATS, ORDERS, 2 * TIMES), 1.0, 6.0, ((2, 16), (4, 2))),
        "vmodes": normal_values(seeds[1], (LEV, KMODES), LEV ** -0.5, 1.25),
        "owner_map": jax.random.permutation(seeds[2], ORDERS).astype(jnp.int32),
        "hough_table": normal_values(seeds[3], (KMODES, ORDERS * HOUGH, 3 * LATS), (3 * LATS) ** -0.5, 0.125, ((0, 2), (1, 16))),
        "keep_mask": place_ends((jax.random.randint(seeds[4], (KMODES, ORDERS * HOUGH), 0, 4) < 3).astype(jnp.int32), jax.random.fold_in(seeds[4], 1), 0, 1),
    }


def reference(fields, vmodes, owner_map, hough_table, keep_mask):
    projected = jnp.einsum('vlamc,lk->vkamc', fields.astype(jnp.float32), vmodes.astype(jnp.float32)).astype(jnp.bfloat16)
    variables, kmodes, lat_count, orders, span_cols = projected.shape
    hough_modes = hough_table.shape[1] // orders

    def one_order(pair_item):
        order_index, slot_index = pair_item
        chosen = lax.dynamic_index_in_dim(projected, order_index, 3, keepdims=False)
        chosen = jnp.transpose(chosen, (1, 0, 2, 3)).reshape(kmodes, variables * lat_count, span_cols)
        row_start = (slot_index * hough_modes).astype(jnp.int32)
        table_rows = lax.dynamic_slice_in_dim(hough_table, row_start, hough_modes, 1).astype(jnp.float32)
        keep_rows = lax.dynamic_slice_in_dim(keep_mask, row_start, hough_modes, 1).astype(jnp.float32)
        coefficients = jnp.einsum('knj,kjc->knc', table_rows, chosen.astype(jnp.float32))
        kept = (coefficients * keep_rows[:, :, None]).astype(jnp.bfloat16)
        synthesis = jnp.einsum('knj,knc->kjc', table_rows, kept.astype(jnp.float32))
        return synthesis.astype(jnp.bfloat16).reshape(kmodes, variables, lat_count, span_cols)

    pieces = lax.map(one_order, (jnp.arange(orders, dtype=jnp.int32), owner_map.astype(jnp.int32)))
    return jnp.transpose(pieces, (1, 2, 3, 0, 4))
```

```python
import jax
import jax.numpy as jnp
from jax import lax
from jax.sharding import PartitionSpec as P

AXES = ("lat", "tm")


def order_of_slot(owner_map):
    ids = jnp.arange(owner_map.shape[0], dtype=jnp.int32)
    hit = owner_map[None, :] == ids[:, None]
    return jnp.sum(jnp.where(hit, ids[None, :], 0), axis=1).astype(jnp.int32)


def body(fields, vmodes, owner_map, hough_table, keep_mask):
    n_lat = lax.axis_size("lat")
    n_tm = lax.axis_size("tm")
    orders = owner_map.shape[0]
    group_size = n_lat // orders
    variables, lev, lat_count, _, span = fields.shape
    kmodes = vmodes.shape[1]
    k_loc = kmodes // n_tm
    vm = vmodes.reshape(lev, n_tm, k_loc)
    projected = jnp.einsum(
        "vlamc,lus->muvsac", fields, vm, preferred_element_type=jnp.float32
    ).astype(jnp.bfloat16)
    dest_order = order_of_slot(owner_map)[jnp.arange(n_lat, dtype=jnp.int32) // group_size]
    outgoing = jnp.take(projected, dest_order, axis=0)
    outgoing = outgoing.reshape(n_lat * n_tm, -1)
    incoming = lax.all_to_all(outgoing, AXES, 0, 0, tiled=True)
    incoming = incoming.reshape(n_lat, n_tm, variables, k_loc, lat_count, span)
    columns = incoming.transpose(3, 2, 0, 4, 1, 5).reshape(
        k_loc, variables * n_lat * lat_count, n_tm * span
    )
    coefficients = jnp.einsum(
        "knj,kjc->knc", hough_table, columns, preferred_element_type=jnp.float32
    )
    kept = (coefficients * keep_mask.astype(jnp.float32)[:, :, None]).astype(jnp.bfloat16)
    synth = jnp.einsum("knj,knc->kjc", hough_table, kept, preferred_element_type=jnp.float32)
    synth = synth.reshape(k_loc, variables, n_lat, lat_count, n_tm, span)
    synth = synth.transpose(2, 4, 0, 1, 3, 5)
    if group_size == 1:
        synth = synth.astype(jnp.bfloat16)
    returned = lax.all_to_all(synth.reshape(n_lat * n_tm, -1), AXES, 0, 0, tiled=True)
    returned = returned.reshape(orders, group_size, n_tm, k_loc, variables, lat_count, span)
    returned = returned.sum(axis=1) if group_size > 1 else returned[:, 0]
    result = jnp.take(returned, owner_map, axis=0)
    result = result.reshape(orders, kmodes, variables, lat_count, span)
    return result.transpose(1, 2, 3, 0, 4).astype(jnp.bfloat16)


def solution(mesh):
    in_specs = (P(None, None, "lat", None, "tm"), P(), P(), P("tm", "lat", None), P("tm", "lat"))
    out_specs = P(None, None, "lat", None, "tm")
    return jax.shard_map(body, mesh=mesh, in_specs=in_specs, out_specs=out_specs, check_vma=False)
```

```python
import jax
import jax.numpy as jnp
from jax import lax
from jax.sharding import PartitionSpec as P

AXES = ("lat", "tm")


def order_of_slot(owner_map):
    ids = jnp.arange(owner_map.shape[0], dtype=jnp.int32)
    hit = owner_map[None, :] == ids[:, None]
    return jnp.sum(jnp.where(hit, ids[None, :], 0), axis=1).astype(jnp.int32)


def body(fields, vmodes, owner_map, hough_table, keep_mask):
    n_lat = lax.axis_size("lat")
    n_tm = lax.axis_size("tm")
    orders = owner_map.shape[0]
    group_size = n_lat // orders
    variables, lev, lat_count, _, span = fields.shape
    kmodes = vmodes.shape[1]
    k_loc = kmodes // n_tm
    block = lat_count * span
    flat = fields.transpose(3, 0, 1, 2, 4).reshape(orders, variables, lev, block)
    dest_order = order_of_slot(owner_map)[jnp.arange(n_lat, dtype=jnp.int32) // group_size]
    picked = jnp.take(flat, dest_order, axis=0, mode="clip")
    vm = vmodes.reshape(lev, n_tm, k_loc)
    outgoing = jnp.einsum(
        "jvlx,lus->jusvx", picked, vm, preferred_element_type=jnp.float32
    ).astype(jnp.bfloat16)
    outgoing = outgoing.reshape(n_lat * n_tm, k_loc * variables, block)
    incoming = lax.all_to_all(outgoing, AXES, 0, 0, tiled=True)
    incoming = incoming.reshape(n_lat, n_tm, k_loc, variables, lat_count, span)
    columns = incoming.transpose(2, 3, 0, 4, 1, 5).reshape(
        k_loc, variables * n_lat * lat_count, n_tm * span
    )
    coefficients = jnp.einsum(
        "knj,kjc->knc", hough_table, columns, preferred_element_type=jnp.float32
    )
    kept = (coefficients * keep_mask.astype(jnp.float32)[:, :, None]).astype(jnp.bfloat16)
    synth = jnp.einsum("knj,knc->kjc", hough_table, kept, preferred_element_type=jnp.float32)
    synth = synth.reshape(k_loc, variables, n_lat, lat_count, n_tm, span)
    synth = synth.transpose(2, 4, 0, 1, 3, 5)
    if group_size == 1:
        synth = synth.astype(jnp.bfloat16)
    synth = synth.reshape(n_lat * n_tm, k_loc * variables, block)
    returned = lax.all_to_all(synth, AXES, 0, 0, tiled=True)
    returned = returned.reshape(orders, group_size, n_tm, k_loc, variables, lat_count, span)
    returned = returned.sum(axis=1) if group_size > 1 else returned[:, 0]
    result = jnp.take(returned, owner_map, axis=0, mode="clip")
    result = result.reshape(orders, kmodes, variables, lat_count, span)
    return result.transpose(1, 2, 3, 0, 4).astype(jnp.bfloat16)


def solution(mesh):
    in_specs = (P(None, None, "lat", None, "tm"), P(), P(), P("tm", "lat", None), P("tm", "lat"))
    out_specs = P(None, None, "lat", None, "tm")
    return jax.shard_map(body, mesh=mesh, in_specs=in_specs, out_specs=out_specs, check_vma=False)
```

```python
import jax
import jax.numpy as jnp
from jax import lax
from jax.sharding import PartitionSpec as P

AXES = ("lat", "tm")


def order_of_slot(owner_map):
    ids = jnp.arange(owner_map.shape[0], dtype=jnp.int32)
    hit = owner_map[None, :] == ids[:, None]
    return jnp.sum(jnp.where(hit, ids[None, :], 0), axis=1).astype(jnp.int32)


def body(fields, vmodes, owner_map, hough_table, keep_mask):
    n_lat = lax.axis_size("lat")
    n_tm = lax.axis_size("tm")
    orders = owner_map.shape[0]
    group_size = n_lat // orders
    variables, lev, lat_count, _, span = fields.shape
    kmodes = vmodes.shape[1]
    k_loc = kmodes // n_tm
    block = lat_count * span
    flat = fields.transpose(3, 0, 1, 4, 2).reshape(orders, variables, lev, block)
    dest_order = order_of_slot(owner_map)[jnp.arange(n_lat, dtype=jnp.int32) // group_size]
    picked = jnp.take(flat, dest_order, axis=0, mode="clip")
    vm = vmodes.reshape(lev, n_tm, k_loc)
    outgoing = jnp.einsum(
        "jvlx,lus->jusvx", picked, vm, preferred_element_type=jnp.float32
    ).astype(jnp.bfloat16)
    outgoing = outgoing.reshape(n_lat * n_tm, k_loc * variables, block)
    incoming = lax.all_to_all(outgoing, AXES, 0, 0, tiled=True)
    incoming = incoming.reshape(n_lat, n_tm, k_loc, variables, span, lat_count)
    columns = incoming.transpose(2, 1, 4, 3, 0, 5).reshape(
        k_loc, n_tm * span, variables * n_lat * lat_count
    )
    coefficients = jnp.einsum(
        "knj,kcj->knc", hough_table, columns, preferred_element_type=jnp.float32
    )
    kept = (coefficients * keep_mask.astype(jnp.float32)[:, :, None]).astype(jnp.bfloat16)
    synth = jnp.einsum("knj,knc->kcj", hough_table, kept, preferred_element_type=jnp.float32)
    synth = synth.reshape(k_loc, n_tm, span, variables, n_lat, lat_count)
    synth = synth.transpose(4, 1, 0, 3, 2, 5)
    if group_size == 1:
        synth = synth.astype(jnp.bfloat16)
    synth = synth.reshape(n_lat * n_tm, k_loc * variables, block)
    returned = lax.all_to_all(synth, AXES, 0, 0, tiled=True)
    returned = returned.reshape(orders, group_size, n_tm, k_loc, variables, span, lat_count)
    returned = returned.sum(axis=1) if group_size > 1 else returned[:, 0]
    result = jnp.take(returned, owner_map, axis=0, mode="clip")
    result = result.reshape(orders, kmodes, variables, span, lat_count)
    return result.transpose(1, 2, 4, 0, 3).astype(jnp.bfloat16)


def solution(mesh):
    in_specs = (P(None, None, "lat", None, "tm"), P(), P(), P("tm", "lat", None), P("tm", "lat"))
    out_specs = P(None, None, "lat", None, "tm")
    return jax.shard_map(body, mesh=mesh, in_specs=in_specs, out_specs=out_specs, check_vma=False)
```

```python
import math

import jax
import jax.numpy as jnp
from jax import lax
from jax.sharding import PartitionSpec as P

AXES = ("lat", "tm")
CHUNKS = 4


def order_of_slot(owner_map):
    ids = jnp.arange(owner_map.shape[0], dtype=jnp.int32)
    hit = owner_map[None, :] == ids[:, None]
    return jnp.sum(jnp.where(hit, ids[None, :], 0), axis=1).astype(jnp.int32)


def body(fields, vmodes, owner_map, hough_table, keep_mask):
    n_lat = lax.axis_size("lat")
    n_tm = lax.axis_size("tm")
    n_dev = n_lat * n_tm
    orders = owner_map.shape[0]
    group_size = n_lat // orders
    variables, lev, lat_count, _, span = fields.shape
    kmodes = vmodes.shape[1]
    k_loc = kmodes // n_tm
    chunks = math.gcd(k_loc, CHUNKS)
    k_chunk = k_loc // chunks
    block = lat_count * span
    flat = fields.transpose(3, 0, 1, 4, 2).reshape(orders, variables, lev, block)
    dest_order = order_of_slot(owner_map)[jnp.arange(n_lat, dtype=jnp.int32) // group_size]
    picked = jnp.take(flat, dest_order, axis=0, mode="clip")
    vm = vmodes.reshape(lev, n_tm, k_loc)
    projected = jnp.einsum(
        "jvlx,lus->jusvx", picked, vm, preferred_element_type=jnp.float32
    ).astype(jnp.bfloat16)
    mask = keep_mask.astype(jnp.float32)
    pieces = []
    for q in range(chunks):
        ks = slice(q * k_chunk, (q + 1) * k_chunk)
        outgoing = projected[:, :, ks].reshape(n_dev, k_chunk * variables, block)
        incoming = lax.all_to_all(outgoing, AXES, 0, 0, tiled=True)
        incoming = incoming.reshape(n_lat, n_tm, k_chunk, variables, span, lat_count)
        columns = incoming.transpose(2, 1, 4, 3, 0, 5).reshape(
            k_chunk, n_tm * span, variables * n_lat * lat_count
        )
        table = hough_table[ks]
        coefficients = jnp.einsum(
            "knj,kcj->knc", table, columns, preferred_element_type=jnp.float32
        )
        kept = (coefficients * mask[ks][:, :, None]).astype(jnp.bfloat16)
        synth = jnp.einsum("knj,knc->kcj", table, kept, preferred_element_type=jnp.float32)
        synth = synth.reshape(k_chunk, n_tm, span, variables, n_lat, lat_count)
        synth = synth.transpose(4, 1, 0, 3, 2, 5)
        if group_size == 1:
            synth = synth.astype(jnp.bfloat16)
        synth = synth.reshape(n_dev, k_chunk * variables, block)
        returned = lax.all_to_all(synth, AXES, 0, 0, tiled=True)
        pieces.append(returned.reshape(n_lat, n_tm, k_chunk, variables, span, lat_count))
    returned = jnp.concatenate(pieces, axis=2)
    returned = returned.reshape(orders, group_size, n_tm, k_loc, variables, span, lat_count)
    returned = returned.sum(axis=1) if group_size > 1 else returned[:, 0]
    result = jnp.take(returned, owner_map, axis=0, mode="clip")
    result = result.reshape(orders, kmodes, variables, span, lat_count)
    return result.transpose(1, 2, 4, 0, 3).astype(jnp.bfloat16)


def solution(mesh):
    in_specs = (P(None, None, "lat", None, "tm"), P(), P(), P("tm", "lat", None), P("tm", "lat"))
    out_specs = P(None, None, "lat", None, "tm")
    return jax.shard_map(body, mesh=mesh, in_specs=in_specs, out_specs=out_specs, check_vma=False)
```

```python
import math

import jax
import jax.numpy as jnp
from jax import lax
from jax.sharding import PartitionSpec as P

AXES = ("lat", "tm")
CHUNKS = 2


def order_of_slot(owner_map):
    ids = jnp.arange(owner_map.shape[0], dtype=jnp.int32)
    hit = owner_map[None, :] == ids[:, None]
    return jnp.sum(jnp.where(hit, ids[None, :], 0), axis=1).astype(jnp.int32)


def body(fields, vmodes, owner_map, hough_table, keep_mask):
    n_lat = lax.axis_size("lat")
    n_tm = lax.axis_size("tm")
    n_dev = n_lat * n_tm
    orders = owner_map.shape[0]
    group_size = n_lat // orders
    variables, lev, lat_count, _, span = fields.shape
    kmodes = vmodes.shape[1]
    k_loc = kmodes // n_tm
    chunks = math.gcd(k_loc, CHUNKS)
    k_chunk = k_loc // chunks
    block = lat_count * span
    flat = fields.transpose(3, 0, 1, 4, 2).reshape(orders, variables, lev, block)
    dest_order = order_of_slot(owner_map)[jnp.arange(n_lat, dtype=jnp.int32) // group_size]
    picked = jnp.take(flat, dest_order, axis=0, mode="clip")
    vm = vmodes.reshape(lev, n_tm, k_loc)
    projected = jnp.einsum(
        "jvlx,lus->jusvx", picked, vm, preferred_element_type=jnp.float32
    ).astype(jnp.bfloat16)
    mask = keep_mask.astype(jnp.float32)
    pieces = []
    for q in range(chunks):
        ks = slice(q * k_chunk, (q + 1) * k_chunk)
        outgoing = projected[:, :, ks].reshape(n_dev, k_chunk * variables, block)
        incoming = lax.all_to_all(outgoing, AXES, 0, 0, tiled=True)
        incoming = incoming.reshape(n_lat, n_tm, k_chunk, variables, span, lat_count)
        columns = incoming.transpose(2, 1, 4, 3, 0, 5).reshape(
            k_chunk, n_tm * span, variables * n_lat * lat_count
        )
        table = hough_table[ks]
        coefficients = jnp.einsum(
            "knj,kcj->knc", table, columns, preferred_element_type=jnp.float32
        )
        kept = (coefficients * mask[ks][:, :, None]).astype(jnp.bfloat16)
        synth = jnp.einsum("knj,knc->kcj", table, kept, preferred_element_type=jnp.float32)
        synth = synth.reshape(k_chunk, n_tm, span, variables, n_lat, lat_count)
        synth = synth.transpose(4, 1, 0, 3, 2, 5)
        if group_size == 1:
            synth = synth.astype(jnp.bfloat16)
        synth = synth.reshape(n_dev, k_chunk * variables, block)
        returned = lax.all_to_all(synth, AXES, 0, 0, tiled=True)
        pieces.append(returned.reshape(n_lat, n_tm, k_chunk, variables, span, lat_count))
    returned = jnp.concatenate(pieces, axis=2)
    returned = returned.reshape(orders, group_size, n_tm, k_loc, variables, span, lat_count)
    returned = returned.sum(axis=1) if group_size > 1 else returned[:, 0]
    result = jnp.take(returned, owner_map, axis=0, mode="clip")
    result = result.reshape(orders, kmodes, variables, span, lat_count)
    return result.transpose(1, 2, 4, 0, 3).astype(jnp.bfloat16)


def solution(mesh):
    in_specs = (P(None, None, "lat", None, "tm"), P(), P(), P("tm", "lat", None), P("tm", "lat"))
    out_specs = P(None, None, "lat", None, "tm")
    return jax.shard_map(body, mesh=mesh, in_specs=in_specs, out_specs=out_specs, check_vma=False)
```

```python
import jax
import jax.numpy as jnp
from jax import lax
from jax.experimental import pallas as pl
from jax.sharding import PartitionSpec as P

AXES = ("lat", "tm")


def order_of_slot(owner_map):
    ids = jnp.arange(owner_map.shape[0], dtype=jnp.int32)
    hit = owner_map[None, :] == ids[:, None]
    return jnp.sum(jnp.where(hit, ids[None, :], 0), axis=1).astype(jnp.int32)


def filter_kernel(t_ref, x_ref, m_ref, o_ref):
    table = t_ref[0]
    coefficients = lax.dot_general(
        x_ref[0], table, (((1,), (1,)), ((), ())), preferred_element_type=jnp.float32
    )
    kept = (coefficients * m_ref[0]).astype(jnp.bfloat16)
    synth = jnp.dot(kept, table, preferred_element_type=jnp.float32)
    o_ref[0] = synth.astype(o_ref.dtype)


def filter_rows(hough_table, columns, mask, out_dtype):
    k_loc, rows, width = hough_table.shape
    cols = columns.shape[1]
    return pl.pallas_call(
        filter_kernel,
        grid=(k_loc,),
        in_specs=[
            pl.BlockSpec((1, rows, width), lambda k: (k, 0, 0)),
            pl.BlockSpec((1, cols, width), lambda k: (k, 0, 0)),
            pl.BlockSpec((1, 1, rows), lambda k: (k, 0, 0)),
        ],
        out_specs=pl.BlockSpec((1, cols, width), lambda k: (k, 0, 0)),
        out_shape=jax.ShapeDtypeStruct((k_loc, cols, width), out_dtype),
    )(hough_table, columns, mask)


def body(fields, vmodes, owner_map, hough_table, keep_mask):
    n_lat = lax.axis_size("lat")
    n_tm = lax.axis_size("tm")
    orders = owner_map.shape[0]
    group_size = n_lat // orders
    variables, lev, lat_count, _, span = fields.shape
    kmodes = vmodes.shape[1]
    k_loc = kmodes // n_tm
    block = lat_count * span
    flat = fields.transpose(3, 0, 1, 4, 2).reshape(orders, variables, lev, block)
    dest_order = order_of_slot(owner_map)[jnp.arange(n_lat, dtype=jnp.int32) // group_size]
    picked = jnp.take(flat, dest_order, axis=0, mode="clip")
    vm = vmodes.reshape(lev, n_tm, k_loc)
    outgoing = jnp.einsum(
        "jvlx,lus->jusvx", picked, vm, preferred_element_type=jnp.float32
    ).astype(jnp.bfloat16)
    outgoing = outgoing.reshape(n_lat * n_tm, k_loc * variables, block)
    incoming = lax.all_to_all(outgoing, AXES, 0, 0, tiled=True)
    incoming = incoming.reshape(n_lat, n_tm, k_loc, variables, span, lat_count)
    columns = incoming.transpose(2, 1, 4, 3, 0, 5).reshape(
        k_loc, n_tm * span, variables * n_lat * lat_count
    )
    mask = keep_mask.astype(jnp.float32).reshape(k_loc, 1, -1)
    out_dtype = jnp.bfloat16 if group_size == 1 else jnp.float32
    synth = filter_rows(hough_table, columns, mask, out_dtype)
    synth = synth.reshape(k_loc, n_tm, span, variables, n_lat, lat_count)
    synth = synth.transpose(4, 1, 0, 3, 2, 5)
    synth = synth.reshape(n_lat * n_tm, k_loc * variables, block)
    returned = lax.all_to_all(synth, AXES, 0, 0, tiled=True)
    returned = returned.reshape(orders, group_size, n_tm, k_loc, variables, span, lat_count)
    returned = returned.sum(axis=1) if group_size > 1 else returned[:, 0]
    result = jnp.take(returned, owner_map, axis=0, mode="clip")
    result = result.reshape(orders, kmodes, variables, span, lat_count)
    return result.transpose(1, 2, 4, 0, 3).astype(jnp.bfloat16)


def solution(mesh):
    in_specs = (P(None, None, "lat", None, "tm"), P(), P(), P("tm", "lat", None), P("tm", "lat"))
    out_specs = P(None, None, "lat", None, "tm")
    return jax.shard_map(body, mesh=mesh, in_specs=in_specs, out_specs=out_specs, check_vma=False)
```

```python
import jax
import jax.numpy as jnp
from jax import lax
from jax.experimental import pallas as pl
from jax.experimental.pallas import tpu as pltpu
from jax.sharding import PartitionSpec as P

AXES = ("lat", "tm")


def order_of_slot(owner_map):
    ids = jnp.arange(owner_map.shape[0], dtype=jnp.int32)
    hit = owner_map[None, :] == ids[:, None]
    return jnp.sum(jnp.where(hit, ids[None, :], 0), axis=1).astype(jnp.int32)


def filter_kernel(t_ref, r_ref, m_ref, o_ref, x_scr, y_scr):
    n_lat, n_tm, _, variables, span, lat_count = r_ref.shape
    seg = n_lat * lat_count
    for t in range(n_tm):
        for v in range(variables):
            for i in range(n_lat):
                x_scr[pl.ds(t * span, span), pl.ds(v * seg + i * lat_count, lat_count)] = r_ref[i, t, 0, v]
    table = t_ref[0]
    coefficients = lax.dot_general(
        x_scr[...], table, (((1,), (1,)), ((), ())), preferred_element_type=jnp.float32
    )
    kept = (coefficients * m_ref[0]).astype(jnp.bfloat16)
    synth = jnp.dot(kept, table, preferred_element_type=jnp.float32)
    y_scr[...] = synth.astype(y_scr.dtype)
    for t in range(n_tm):
        for v in range(variables):
            for i in range(n_lat):
                o_ref[i, t, 0, v] = y_scr[pl.ds(t * span, span), pl.ds(v * seg + i * lat_count, lat_count)]


def filter_rows(hough_table, received, mask, out_dtype):
    k_loc, rows, width = hough_table.shape
    n_lat, n_tm, _, variables, span, lat_count = received.shape
    cols = n_tm * span
    block = (n_lat, n_tm, 1, variables, span, lat_count)
    return pl.pallas_call(
        filter_kernel,
        grid=(k_loc,),
        in_specs=[
            pl.BlockSpec((1, rows, width), lambda k: (k, 0, 0)),
            pl.BlockSpec(block, lambda k: (0, 0, k, 0, 0, 0)),
            pl.BlockSpec((1, 1, rows), lambda k: (k, 0, 0)),
        ],
        out_specs=pl.BlockSpec(block, lambda k: (0, 0, k, 0, 0, 0)),
        out_shape=jax.ShapeDtypeStruct(received.shape, out_dtype),
        scratch_shapes=[pltpu.VMEM((cols, width), jnp.bfloat16), pltpu.VMEM((cols, width), out_dtype)],
    )(hough_table, received, mask)


def body(fields, vmodes, owner_map, hough_table, keep_mask):
    n_lat = lax.axis_size("lat")
    n_tm = lax.axis_size("tm")
    orders = owner_map.shape[0]
    group_size = n_lat // orders
    variables, lev, lat_count, _, span = fields.shape
    kmodes = vmodes.shape[1]
    k_loc = kmodes // n_tm
    block = lat_count * span
    flat = fields.transpose(3, 0, 1, 4, 2).reshape(orders, variables, lev, block)
    dest_order = order_of_slot(owner_map)[jnp.arange(n_lat, dtype=jnp.int32) // group_size]
    picked = jnp.take(flat, dest_order, axis=0, mode="clip")
    vm = vmodes.reshape(lev, n_tm, k_loc)
    outgoing = jnp.einsum(
        "jvlx,lus->jusvx", picked, vm, preferred_element_type=jnp.float32
    ).astype(jnp.bfloat16)
    outgoing = outgoing.reshape(n_lat * n_tm, k_loc * variables, block)
    incoming = lax.all_to_all(outgoing, AXES, 0, 0, tiled=True)
    incoming = incoming.reshape(n_lat, n_tm, k_loc, variables, span, lat_count)
    mask = keep_mask.astype(jnp.float32).reshape(k_loc, 1, -1)
    out_dtype = jnp.bfloat16 if group_size == 1 else jnp.float32
    synth = filter_rows(hough_table, incoming, mask, out_dtype)
    synth = synth.reshape(n_lat * n_tm, k_loc * variables, block)
    returned = lax.all_to_all(synth, AXES, 0, 0, tiled=True)
    returned = returned.reshape(orders, group_size, n_tm, k_loc, variables, span, lat_count)
    returned = returned.sum(axis=1) if group_size > 1 else returned[:, 0]
    result = jnp.take(returned, owner_map, axis=0, mode="clip")
    result = result.reshape(orders, kmodes, variables, span, lat_count)
    return result.transpose(1, 2, 4, 0, 3).astype(jnp.bfloat16)


def solution(mesh):
    in_specs = (P(None, None, "lat", None, "tm"), P(), P(), P("tm", "lat", None), P("tm", "lat"))
    out_specs = P(None, None, "lat", None, "tm")
    return jax.shard_map(body, mesh=mesh, in_specs=in_specs, out_specs=out_specs, check_vma=False)
```

```python
import functools

import jax
import jax.numpy as jnp
from jax import lax
from jax.experimental import pallas as pl
from jax.experimental.pallas import tpu as pltpu
from jax.sharding import PartitionSpec as P

AXES = ("lat", "tm")


def order_of_slot(owner_map):
    ids = jnp.arange(owner_map.shape[0], dtype=jnp.int32)
    hit = owner_map[None, :] == ids[:, None]
    return jnp.sum(jnp.where(hit, ids[None, :], 0), axis=1).astype(jnp.int32)


def filter_kernel(variables, t_ref, r_ref, m_ref, o_ref, x_scr, y_scr):
    n_lat, n_tm, _, span, lanes = r_ref.shape
    lat_count = lanes // variables
    seg = n_lat * lat_count
    for t in range(n_tm):
        for v in range(variables):
            for i in range(n_lat):
                x_scr[pl.ds(t * span, span), pl.ds(v * seg + i * lat_count, lat_count)] = r_ref[
                    i, t, 0, :, pl.ds(v * lat_count, lat_count)
                ]
    table = t_ref[0]
    coefficients = lax.dot_general(
        x_scr[...], table, (((1,), (1,)), ((), ())), preferred_element_type=jnp.float32
    )
    kept = (coefficients * m_ref[0]).astype(jnp.bfloat16)
    synth = jnp.dot(kept, table, preferred_element_type=jnp.float32)
    y_scr[...] = synth.astype(y_scr.dtype)
    for t in range(n_tm):
        for v in range(variables):
            for i in range(n_lat):
                o_ref[i, t, 0, :, pl.ds(v * lat_count, lat_count)] = y_scr[
                    pl.ds(t * span, span), pl.ds(v * seg + i * lat_count, lat_count)
                ]


def filter_rows(hough_table, received, mask, out_dtype, variables):
    k_loc, rows, width = hough_table.shape
    n_lat, n_tm, _, span, lanes = received.shape
    cols = n_tm * span
    block = (n_lat, n_tm, 1, span, lanes)
    return pl.pallas_call(
        functools.partial(filter_kernel, variables),
        grid=(k_loc,),
        in_specs=[
            pl.BlockSpec((1, rows, width), lambda k: (k, 0, 0)),
            pl.BlockSpec(block, lambda k: (0, 0, k, 0, 0)),
            pl.BlockSpec((1, 1, rows), lambda k: (k, 0, 0)),
        ],
        out_specs=pl.BlockSpec(block, lambda k: (0, 0, k, 0, 0)),
        out_shape=jax.ShapeDtypeStruct(received.shape, out_dtype),
        scratch_shapes=[pltpu.VMEM((cols, width), jnp.bfloat16), pltpu.VMEM((cols, width), out_dtype)],
    )(hough_table, received, mask)


def body(fields, vmodes, owner_map, hough_table, keep_mask):
    n_lat = lax.axis_size("lat")
    n_tm = lax.axis_size("tm")
    orders = owner_map.shape[0]
    group_size = n_lat // orders
    variables, lev, lat_count, _, span = fields.shape
    kmodes = vmodes.shape[1]
    k_loc = kmodes // n_tm
    by_order = fields.transpose(3, 0, 1, 4, 2)
    dest_order = order_of_slot(owner_map)[jnp.arange(n_lat, dtype=jnp.int32) // group_size]
    picked = jnp.take(by_order, dest_order, axis=0, mode="clip")
    vm = vmodes.reshape(lev, n_tm, k_loc)
    outgoing = jnp.einsum(
        "jvlca,lus->juscva", picked, vm, preferred_element_type=jnp.float32
    ).astype(jnp.bfloat16)
    outgoing = outgoing.reshape(n_lat * n_tm, k_loc * span, variables * lat_count)
    incoming = lax.all_to_all(outgoing, AXES, 0, 0, tiled=True)
    incoming = incoming.reshape(n_lat, n_tm, k_loc, span, variables * lat_count)
    mask = keep_mask.astype(jnp.float32).reshape(k_loc, 1, -1)
    out_dtype = jnp.bfloat16 if group_size == 1 else jnp.float32
    synth = filter_rows(hough_table, incoming, mask, out_dtype, variables)
    synth = synth.reshape(n_lat * n_tm, k_loc * span, variables * lat_count)
    returned = lax.all_to_all(synth, AXES, 0, 0, tiled=True)
    returned = returned.reshape(orders, group_size, n_tm, k_loc, span, variables, lat_count)
    returned = returned.sum(axis=1) if group_size > 1 else returned[:, 0]
    result = jnp.take(returned, owner_map, axis=0, mode="clip")
    result = result.reshape(orders, kmodes, span, variables, lat_count)
    return result.transpose(1, 3, 4, 0, 2).astype(jnp.bfloat16)


def solution(mesh):
    in_specs = (P(None, None, "lat", None, "tm"), P(), P(), P("tm", "lat", None), P("tm", "lat"))
    out_specs = P(None, None, "lat", None, "tm")
    return jax.shard_map(body, mesh=mesh, in_specs=in_specs, out_specs=out_specs, check_vma=False)
```

```python
import jax
import jax.numpy as jnp
from jax import lax
from jax.experimental import pallas as pl
from jax.experimental.pallas import tpu as pltpu
from jax.sharding import PartitionSpec as P

AXES = ("lat", "tm")


def order_of_slot(owner_map):
    ids = jnp.arange(owner_map.shape[0], dtype=jnp.int32)
    hit = owner_map[None, :] == ids[:, None]
    return jnp.sum(jnp.where(hit, ids[None, :], 0), axis=1).astype(jnp.int32)


def filter_kernel(t_ref, r_ref, m_ref, o_ref, x_scr, y_scr):
    n_lat, n_tm, _, variables, span, lat_count = r_ref.shape
    seg = n_lat * lat_count
    for t in range(n_tm):
        for v in range(variables):
            for i in range(n_lat):
                x_scr[pl.ds(t * span, span), pl.ds(v * seg + i * lat_count, lat_count)] = r_ref[i, t, 0, v]
    table = t_ref[0]
    coefficients = lax.dot_general(
        table, x_scr[...], (((1,), (1,)), ((), ())), preferred_element_type=jnp.float32
    )
    kept = (coefficients * m_ref[0]).astype(jnp.bfloat16)
    synth = lax.dot_general(
        kept, table, (((0,), (0,)), ((), ())), preferred_element_type=jnp.float32
    )
    y_scr[...] = synth.astype(y_scr.dtype)
    for t in range(n_tm):
        for v in range(variables):
            for i in range(n_lat):
                o_ref[i, t, 0, v] = y_scr[pl.ds(t * span, span), pl.ds(v * seg + i * lat_count, lat_count)]


def filter_rows(hough_table, received, mask, out_dtype):
    k_loc, rows, width = hough_table.shape
    n_lat, n_tm, _, variables, span, lat_count = received.shape
    cols = n_tm * span
    block = (n_lat, n_tm, 1, variables, span, lat_count)
    return pl.pallas_call(
        filter_kernel,
        grid=(k_loc,),
        in_specs=[
            pl.BlockSpec((1, rows, width), lambda k: (k, 0, 0)),
            pl.BlockSpec(block, lambda k: (0, 0, k, 0, 0, 0)),
            pl.BlockSpec((1, rows, 1), lambda k: (k, 0, 0)),
        ],
        out_specs=pl.BlockSpec(block, lambda k: (0, 0, k, 0, 0, 0)),
        out_shape=jax.ShapeDtypeStruct(received.shape, out_dtype),
        scratch_shapes=[pltpu.VMEM((cols, width), jnp.bfloat16), pltpu.VMEM((cols, width), out_dtype)],
    )(hough_table, received, mask)


def body(fields, vmodes, owner_map, hough_table, keep_mask):
    n_lat = lax.axis_size("lat")
    n_tm = lax.axis_size("tm")
    orders = owner_map.shape[0]
    group_size = n_lat // orders
    variables, lev, lat_count, _, span = fields.shape
    kmodes = vmodes.shape[1]
    k_loc = kmodes // n_tm
    block = lat_count * span
    flat = fields.transpose(3, 0, 1, 4, 2).reshape(orders, variables, lev, block)
    dest_order = order_of_slot(owner_map)[jnp.arange(n_lat, dtype=jnp.int32) // group_size]
    picked = jnp.take(flat, dest_order, axis=0, mode="clip")
    vm = vmodes.reshape(lev, n_tm, k_loc)
    outgoing = jnp.einsum(
        "jvlx,lus->jusvx", picked, vm, preferred_element_type=jnp.float32
    ).astype(jnp.bfloat16)
    outgoing = outgoing.reshape(n_lat * n_tm, k_loc * variables, block)
    incoming = lax.all_to_all(outgoing, AXES, 0, 0, tiled=True)
    incoming = incoming.reshape(n_lat, n_tm, k_loc, variables, span, lat_count)
    mask = keep_mask.astype(jnp.float32).reshape(k_loc, -1, 1)
    out_dtype = jnp.bfloat16 if group_size == 1 else jnp.float32
    synth = filter_rows(hough_table, incoming, mask, out_dtype)
    synth = synth.reshape(n_lat * n_tm, k_loc * variables, block)
    returned = lax.all_to_all(synth, AXES, 0, 0, tiled=True)
    returned = returned.reshape(orders, group_size, n_tm, k_loc, variables, span, lat_count)
    returned = returned.sum(axis=1) if group_size > 1 else returned[:, 0]
    result = jnp.take(returned, owner_map, axis=0, mode="clip")
    result = result.reshape(orders, kmodes, variables, span, lat_count)
    return result.transpose(1, 2, 4, 0, 3).astype(jnp.bfloat16)


def solution(mesh):
    in_specs = (P(None, None, "lat", None, "tm"), P(), P(), P("tm", "lat", None), P("tm", "lat"))
    out_specs = P(None, None, "lat", None, "tm")
    return jax.shard_map(body, mesh=mesh, in_specs=in_specs, out_specs=out_specs, check_vma=False)
```

```python
import jax
import jax.numpy as jnp
from jax import lax
from jax.experimental import pallas as pl
from jax.experimental.pallas import tpu as pltpu
from jax.sharding import PartitionSpec as P

AXES = ("lat", "tm")


def order_of_slot(owner_map):
    ids = jnp.arange(owner_map.shape[0], dtype=jnp.int32)
    hit = owner_map[None, :] == ids[:, None]
    return jnp.sum(jnp.where(hit, ids[None, :], 0), axis=1).astype(jnp.int32)


def filter_kernel(t_ref, r_ref, m_ref, o_ref, x_scr, y_scr):
    n_lat, n_tm, _, variables, span, lat_count = r_ref.shape
    seg = n_lat * lat_count
    for t in range(n_tm):
        for v in range(variables):
            for i in range(n_lat):
                x_scr[pl.ds(t * span, span), pl.ds(v * seg + i * lat_count, lat_count)] = r_ref[i, t, 0, v]
    table = t_ref[0]
    coefficients = lax.dot_general(
        x_scr[...], table, (((1,), (1,)), ((), ())), preferred_element_type=jnp.float32
    )
    kept = (coefficients * m_ref[0]).astype(jnp.bfloat16)
    synth = jnp.dot(kept, table, preferred_element_type=jnp.float32)
    y_scr[...] = synth.astype(y_scr.dtype)
    for t in range(n_tm):
        for v in range(variables):
            for i in range(n_lat):
                o_ref[i, t, 0, v] = y_scr[pl.ds(t * span, span), pl.ds(v * seg + i * lat_count, lat_count)]


def filter_rows(hough_table, received, mask, out_dtype):
    k_loc, rows, width = hough_table.shape
    n_lat, n_tm, _, variables, span, lat_count = received.shape
    cols = n_tm * span
    block = (n_lat, n_tm, 1, variables, span, lat_count)
    return pl.pallas_call(
        filter_kernel,
        grid=(k_loc,),
        in_specs=[
            pl.BlockSpec((1, rows, width), lambda k: (k, 0, 0)),
            pl.BlockSpec(block, lambda k: (0, 0, k, 0, 0, 0)),
            pl.BlockSpec((1, 1, rows), lambda k: (k, 0, 0)),
        ],
        out_specs=pl.BlockSpec(block, lambda k: (0, 0, k, 0, 0, 0)),
        out_shape=jax.ShapeDtypeStruct(received.shape, out_dtype),
        scratch_shapes=[pltpu.VMEM((cols, width), jnp.bfloat16), pltpu.VMEM((cols, width), out_dtype)],
    )(hough_table, received, mask)


def body(fields, vmodes, owner_map, hough_table, keep_mask):
    n_lat = lax.axis_size("lat")
    n_tm = lax.axis_size("tm")
    orders = owner_map.shape[0]
    group_size = n_lat // orders
    variables, lev, lat_count, _, span = fields.shape
    kmodes = vmodes.shape[1]
    k_loc = kmodes // n_tm
    block = lat_count * span
    flat = fields.transpose(3, 0, 1, 4, 2).reshape(orders, variables, lev, block)
    dest_order = order_of_slot(owner_map)[jnp.arange(n_lat, dtype=jnp.int32) // group_size]
    picked = jnp.take(flat, dest_order, axis=0, mode="clip")
    vm = vmodes.reshape(lev, n_tm, k_loc)
    outgoing = jnp.einsum(
        "jvlx,lus->jusvx", picked, vm, preferred_element_type=jnp.float32
    ).astype(jnp.bfloat16)
    outgoing = outgoing.reshape(n_lat * n_tm, k_loc * variables, block)
    incoming = lax.all_to_all(outgoing, AXES, 0, 0, tiled=True)
    incoming = incoming.reshape(n_lat, n_tm, k_loc, variables, span, lat_count)
    mask = keep_mask.astype(jnp.float32).reshape(k_loc, 1, -1)
    out_dtype = jnp.bfloat16 if group_size == 1 else jnp.float32
    synth = filter_rows(hough_table, incoming, mask, out_dtype)
    synth = synth.reshape(n_lat * n_tm, k_loc * variables, block)
    returned = lax.all_to_all(synth, AXES, 0, 0, tiled=True)
    returned = returned.reshape(orders, group_size, n_tm * k_loc * variables, block)
    returned = returned.sum(axis=1) if group_size > 1 else returned[:, 0]
    result = jnp.take(returned, owner_map, axis=0, mode="clip")
    result = result.reshape(orders, kmodes, variables, span, lat_count)
    return result.transpose(1, 2, 4, 0, 3).astype(jnp.bfloat16)


def solution(mesh):
    in_specs = (P(None, None, "lat", None, "tm"), P(), P(), P("tm", "lat", None), P("tm", "lat"))
    out_specs = P(None, None, "lat", None, "tm")
    return jax.shard_map(body, mesh=mesh, in_specs=in_specs, out_specs=out_specs, check_vma=False)
```

```python
import math
import jax
import jax.numpy as jnp
from jax import lax
from jax.experimental import pallas as pl
from jax.experimental.pallas import tpu as pltpu
from jax.sharding import PartitionSpec as P

AXES = ("lat", "tm")
CHUNKS = 2


def order_of_slot(owner_map):
    ids = jnp.arange(owner_map.shape[0], dtype=jnp.int32)
    hit = owner_map[None, :] == ids[:, None]
    return jnp.sum(jnp.where(hit, ids[None, :], 0), axis=1).astype(jnp.int32)


def filter_kernel(t_ref, r_ref, m_ref, o_ref, x_scr, y_scr):
    n_lat, n_tm, _, variables, span, lat_count = r_ref.shape
    seg = n_lat * lat_count
    for t in range(n_tm):
        for v in range(variables):
            for i in range(n_lat):
                x_scr[pl.ds(t * span, span), pl.ds(v * seg + i * lat_count, lat_count)] = r_ref[i, t, 0, v]
    table = t_ref[0]
    coefficients = lax.dot_general(
        x_scr[...], table, (((1,), (1,)), ((), ())), preferred_element_type=jnp.float32
    )
    kept = (coefficients * m_ref[0]).astype(jnp.bfloat16)
    synth = jnp.dot(kept, table, preferred_element_type=jnp.float32)
    y_scr[...] = synth.astype(y_scr.dtype)
    for t in range(n_tm):
        for v in range(variables):
            for i in range(n_lat):
                o_ref[i, t, 0, v] = y_scr[pl.ds(t * span, span), pl.ds(v * seg + i * lat_count, lat_count)]


def filter_rows(hough_table, received, mask, out_dtype, first):
    _, rows, width = hough_table.shape
    k_loc = received.shape[2]
    n_lat, n_tm, _, variables, span, lat_count = received.shape
    cols = n_tm * span
    block = (n_lat, n_tm, 1, variables, span, lat_count)
    return pl.pallas_call(
        filter_kernel,
        grid=(k_loc,),
        in_specs=[
            pl.BlockSpec((1, rows, width), lambda k: (k + first, 0, 0)),
            pl.BlockSpec(block, lambda k: (0, 0, k, 0, 0, 0)),
            pl.BlockSpec((1, 1, rows), lambda k: (k + first, 0, 0)),
        ],
        out_specs=pl.BlockSpec(block, lambda k: (0, 0, k, 0, 0, 0)),
        out_shape=jax.ShapeDtypeStruct(received.shape, out_dtype),
        scratch_shapes=[pltpu.VMEM((cols, width), jnp.bfloat16), pltpu.VMEM((cols, width), out_dtype)],
    )(hough_table, received, mask)


def body(fields, vmodes, owner_map, hough_table, keep_mask):
    n_lat = lax.axis_size("lat")
    n_tm = lax.axis_size("tm")
    orders = owner_map.shape[0]
    group_size = n_lat // orders
    variables, lev, lat_count, _, span = fields.shape
    kmodes = vmodes.shape[1]
    k_loc = kmodes // n_tm
    block = lat_count * span
    flat = fields.transpose(3, 0, 1, 4, 2).reshape(orders, variables, lev, block)
    dest_order = order_of_slot(owner_map)[jnp.arange(n_lat, dtype=jnp.int32) // group_size]
    picked = jnp.take(flat, dest_order, axis=0, mode="clip")
    vm = vmodes.reshape(lev, n_tm, k_loc)
    outgoing = jnp.einsum(
        "jvlx,lus->jusvx", picked, vm, preferred_element_type=jnp.float32
    ).astype(jnp.bfloat16)
    mask = keep_mask.astype(jnp.float32).reshape(k_loc, 1, -1)
    out_dtype = jnp.bfloat16 if group_size == 1 else jnp.float32
    chunks = math.gcd(k_loc, CHUNKS)
    k_chunk = k_loc // chunks
    pieces = []
    for q in range(chunks):
        part = outgoing[:, :, q * k_chunk:(q + 1) * k_chunk]
        part = part.reshape(n_lat * n_tm, k_chunk * variables, block)
        incoming = lax.all_to_all(part, AXES, 0, 0, tiled=True)
        incoming = incoming.reshape(n_lat, n_tm, k_chunk, variables, span, lat_count)
        synth = filter_rows(hough_table, incoming, mask, out_dtype, q * k_chunk)
        synth = synth.reshape(n_lat * n_tm, k_chunk * variables, block)
        back = lax.all_to_all(synth, AXES, 0, 0, tiled=True)
        pieces.append(back.reshape(n_lat * n_tm, k_chunk, variables * block))
    returned = jnp.concatenate(pieces, axis=1) if chunks > 1 else pieces[0]
    returned = returned.reshape(orders, group_size, n_tm * k_loc * variables, block)
    returned = returned.sum(axis=1) if group_size > 1 else returned[:, 0]
    result = jnp.take(returned, owner_map, axis=0, mode="clip")
    result = result.reshape(orders, kmodes, variables, span, lat_count)
    return result.transpose(1, 2, 4, 0, 3).astype(jnp.bfloat16)


def solution(mesh):
    in_specs = (P(None, None, "lat", None, "tm"), P(), P(), P("tm", "lat", None), P("tm", "lat"))
    out_specs = P(None, None, "lat", None, "tm")
    return jax.shard_map(body, mesh=mesh, in_specs=in_specs, out_specs=out_specs, check_vma=False)
```

```python
import math
import jax
import jax.numpy as jnp
from jax import lax
from jax.experimental import pallas as pl
from jax.experimental.pallas import tpu as pltpu
from jax.sharding import PartitionSpec as P


AXES = ("lat", "tm")
CHUNKS = 2


def order_of_slot(owner_map):
    ids = jnp.arange(owner_map.shape[0], dtype=jnp.int32)
    hit = owner_map[None, :] == ids[:, None]
    return jnp.sum(jnp.where(hit, ids[None, :], 0), axis=1).astype(jnp.int32)


def filter_kernel(t_ref, r_ref, m_ref, o_ref, x_scr, y_scr):
    n_lat, n_tm, _, variables, span, lat_count = r_ref.shape
    seg = n_lat * lat_count
    for t in range(n_tm):
        for v in range(variables):
            for i in range(n_lat):
                x_scr[pl.ds(t * span, span), pl.ds(v * seg + i * lat_count, lat_count)] = r_ref[i, t, 0, v]
    table = t_ref[0]
    coefficients = lax.dot_general(
        x_scr[...], table, (((1,), (1,)), ((), ())), preferred_element_type=jnp.float32
    )
    kept = (coefficients * m_ref[0]).astype(jnp.bfloat16)
    synth = jnp.dot(kept, table, preferred_element_type=jnp.float32)
    y_scr[...] = synth.astype(y_scr.dtype)
    for t in range(n_tm):
        for v in range(variables):
            for i in range(n_lat):
                o_ref[i, t, 0, v] = y_scr[pl.ds(t * span, span), pl.ds(v * seg + i * lat_count, lat_count)]


def filter_rows(hough_table, received, mask, out_dtype, first):
    _, rows, width = hough_table.shape
    k_loc = received.shape[2]
    n_lat, n_tm, _, variables, span, lat_count = received.shape
    cols = n_tm * span
    block = (n_lat, n_tm, 1, variables, span, lat_count)
    return pl.pallas_call(
        filter_kernel,
        grid=(k_loc,),
        in_specs=[
            pl.BlockSpec((1, rows, width), lambda k: (k + first, 0, 0)),
            pl.BlockSpec(block, lambda k: (0, 0, k, 0, 0, 0)),
            pl.BlockSpec((1, 1, rows), lambda k: (k + first, 0, 0)),
        ],
        out_specs=pl.BlockSpec(block, lambda k: (0, 0, k, 0, 0, 0)),
        out_shape=jax.ShapeDtypeStruct(received.shape, out_dtype),
        scratch_shapes=[pltpu.VMEM((cols, width), jnp.bfloat16), pltpu.VMEM((cols, width), out_dtype)],
    )(hough_table, received, mask)


def body_inner(fields, vmodes, owner_map, hough_table, keep_mask):
    n_lat = lax.axis_size("lat")
    n_tm = lax.axis_size("tm")
    orders = owner_map.shape[0]
    group_size = n_lat // orders
    variables, lev, lat_count, _, span = fields.shape
    kmodes = vmodes.shape[1]
    k_loc = kmodes // n_tm
    block = lat_count * span
    flat = fields.transpose(3, 0, 1, 4, 2).reshape(orders, variables, lev, block)
    dest_order = order_of_slot(owner_map)[jnp.arange(n_lat, dtype=jnp.int32) // group_size]
    picked = jnp.take(flat, dest_order, axis=0, mode="clip")
    vm = vmodes.reshape(lev, n_tm, k_loc)
    outgoing = jnp.einsum(
        "jvlx,lus->jusvx", picked, vm, preferred_element_type=jnp.float32
    ).astype(jnp.bfloat16)
    mask = keep_mask.astype(jnp.float32).reshape(k_loc, 1, -1)
    out_dtype = jnp.bfloat16 if group_size == 1 else jnp.float32
    chunks = math.gcd(k_loc, CHUNKS)
    k_chunk = k_loc // chunks
    pieces = []
    for q in range(chunks):
        part = outgoing[:, :, q * k_chunk:(q + 1) * k_chunk]
        part = part.reshape(n_lat * n_tm, k_chunk * variables, block)
        incoming = lax.all_to_all(part, AXES, 0, 0, tiled=True)
        incoming = incoming.reshape(n_lat, n_tm, k_chunk, variables, span, lat_count)
        synth = filter_rows(hough_table, incoming, mask, out_dtype, q * k_chunk)
        synth = synth.reshape(n_lat * n_tm, k_chunk * variables, block)
        back = lax.all_to_all(synth, AXES, 0, 0, tiled=True)
        back = back.reshape(orders, group_size, n_tm * k_chunk * variables, block)
        back = back.sum(axis=1) if group_size > 1 else back[:, 0]
        back = jnp.take(back, owner_map, axis=0, mode="clip")
        pieces.append(back.reshape(orders, n_tm, k_chunk, variables, span, lat_count))
    result = jnp.concatenate(pieces, axis=2) if chunks > 1 else pieces[0]
    result = result.reshape(orders, kmodes, variables, span, lat_count)
    return result.transpose(1, 2, 4, 0, 3).astype(jnp.bfloat16)


def solution(mesh):
    in_specs = (P(None, None, "lat", None, "tm"), P(), P(), P("tm", "lat", None), P("tm", "lat"))
    out_specs = P(None, None, "lat", None, "tm")
    return jax.shard_map(body_inner, mesh=mesh, in_specs=in_specs, out_specs=out_specs, check_vma=False)
```

```python
import math
import jax
import jax.numpy as jnp
from jax import lax
from jax.experimental import pallas as pl
from jax.experimental.pallas import tpu as pltpu
from jax.sharding import PartitionSpec as P


AXES = ("lat", "tm")
CHUNKS = 2


def order_of_slot(owner_map):
    ids = jnp.arange(owner_map.shape[0], dtype=jnp.int32)
    hit = owner_map[None, :] == ids[:, None]
    return jnp.sum(jnp.where(hit, ids[None, :], 0), axis=1).astype(jnp.int32)


def filter_kernel(t_ref, r_ref, m_ref, o_ref, x_scr, y_scr):
    n_lat, n_tm, _, variables, span, lat_count = r_ref.shape
    seg = n_lat * lat_count
    for t in range(n_tm):
        for v in range(variables):
            for i in range(n_lat):
                x_scr[pl.ds(t * span, span), pl.ds(v * seg + i * lat_count, lat_count)] = r_ref[i, t, 0, v]
    table = t_ref[0]
    coefficients = lax.dot_general(
        x_scr[...], table, (((1,), (1,)), ((), ())), preferred_element_type=jnp.float32
    )
    kept = (coefficients * m_ref[0]).astype(jnp.bfloat16)
    synth = jnp.dot(kept, table, preferred_element_type=jnp.float32)
    y_scr[...] = synth.astype(y_scr.dtype)
    for t in range(n_tm):
        for v in range(variables):
            for i in range(n_lat):
                o_ref[i, t, 0, v] = y_scr[pl.ds(t * span, span), pl.ds(v * seg + i * lat_count, lat_count)]


def filter_rows(hough_table, received, mask, out_dtype, first):
    _, rows, width = hough_table.shape
    k_loc = received.shape[2]
    n_lat, n_tm, _, variables, span, lat_count = received.shape
    cols = n_tm * span
    block = (n_lat, n_tm, 1, variables, span, lat_count)
    return pl.pallas_call(
        filter_kernel,
        grid=(k_loc,),
        in_specs=[
            pl.BlockSpec((1, rows, width), lambda k: (k + first, 0, 0)),
            pl.BlockSpec(block, lambda k: (0, 0, k, 0, 0, 0)),
            pl.BlockSpec((1, 1, rows), lambda k: (k + first, 0, 0)),
        ],
        out_specs=pl.BlockSpec(block, lambda k: (0, 0, k, 0, 0, 0)),
        out_shape=jax.ShapeDtypeStruct(received.shape, out_dtype),
        scratch_shapes=[pltpu.VMEM((cols, width), jnp.bfloat16), pltpu.VMEM((cols, width), out_dtype)],
    )(hough_table, received, mask)


def body_inner(fields, vmodes, owner_map, hough_table, keep_mask):
    n_lat = lax.axis_size("lat")
    n_tm = lax.axis_size("tm")
    orders = owner_map.shape[0]
    group_size = n_lat // orders
    variables, _, lat_count, _, span = fields.shape
    kmodes = vmodes.shape[1]
    k_loc = kmodes // n_tm
    block = lat_count * span
    by_order = fields.transpose(3, 0, 1, 4, 2)
    dest_order = order_of_slot(owner_map)[jnp.arange(n_lat, dtype=jnp.int32) // group_size]
    projected = jnp.einsum(
        "mvlca,lk->mkvca", by_order, vmodes, preferred_element_type=jnp.float32
    ).astype(jnp.bfloat16)
    projected = projected.reshape(orders, n_tm, k_loc, variables, span, lat_count)
    mask = keep_mask.astype(jnp.float32).reshape(k_loc, 1, -1)
    out_dtype = jnp.bfloat16 if group_size == 1 else jnp.float32
    chunks = math.gcd(k_loc, CHUNKS)
    k_chunk = k_loc // chunks
    pieces = []
    for q in range(chunks):
        part = projected[:, :, q * k_chunk:(q + 1) * k_chunk]
        part = part.reshape(orders, n_tm, k_chunk, variables, block)
        part = jnp.take(part, dest_order, axis=0, mode="clip")
        part = part.reshape(n_lat * n_tm, k_chunk * variables, block)
        incoming = lax.all_to_all(part, AXES, 0, 0, tiled=True)
        incoming = incoming.reshape(n_lat, n_tm, k_chunk, variables, span, lat_count)
        synth = filter_rows(hough_table, incoming, mask, out_dtype, q * k_chunk)
        synth = synth.reshape(n_lat * n_tm, k_chunk * variables, block)
        back = lax.all_to_all(synth, AXES, 0, 0, tiled=True)
        back = back.reshape(orders, group_size, n_tm * k_chunk * variables, block)
        back = back.sum(axis=1) if group_size > 1 else back[:, 0]
        back = jnp.take(back, owner_map, axis=0, mode="clip")
        pieces.append(back.reshape(orders, n_tm, k_chunk, variables, span, lat_count))
    result = jnp.concatenate(pieces, axis=2) if chunks > 1 else pieces[0]
    result = result.reshape(orders, kmodes, variables, span, lat_count)
    return result.transpose(1, 2, 4, 0, 3).astype(jnp.bfloat16)


def solution(mesh):
    in_specs = (P(None, None, "lat", None, "tm"), P(), P(), P("tm", "lat", None), P("tm", "lat"))
    out_specs = P(None, None, "lat", None, "tm")
    return jax.shard_map(body_inner, mesh=mesh, in_specs=in_specs, out_specs=out_specs, check_vma=False)
```

```python
import jax
import jax.numpy as jnp
from jax import lax
from jax.experimental import pallas as pl
from jax.experimental.pallas import tpu as pltpu
from jax.sharding import PartitionSpec as P


AXES = ("lat", "tm")


def order_of_slot(owner_map):
    ids = jnp.arange(owner_map.shape[0], dtype=jnp.int32)
    hit = owner_map[None, :] == ids[:, None]
    return jnp.sum(jnp.where(hit, ids[None, :], 0), axis=1).astype(jnp.int32)


def filter_kernel(t_ref, r_ref, m_ref, o_ref, x_scr, y_scr):
    n_lat, n_tm, _, variables, span, lat_count = r_ref.shape
    seg = n_lat * lat_count
    for t in range(n_tm):
        for v in range(variables):
            for i in range(n_lat):
                x_scr[pl.ds(t * span, span), pl.ds(v * seg + i * lat_count, lat_count)] = r_ref[i, t, 0, v]
    table = t_ref[0]
    coefficients = lax.dot_general(
        x_scr[...], table, (((1,), (1,)), ((), ())), preferred_element_type=jnp.float32
    )
    kept = (coefficients * m_ref[0]).astype(jnp.bfloat16)
    synth = jnp.dot(kept, table, preferred_element_type=jnp.float32)
    y_scr[...] = synth.astype(y_scr.dtype)
    for t in range(n_tm):
        for v in range(variables):
            for i in range(n_lat):
                o_ref[i, t, 0, v] = y_scr[pl.ds(t * span, span), pl.ds(v * seg + i * lat_count, lat_count)]


def filter_rows(hough_table, received, mask, out_dtype, first):
    _, rows, width = hough_table.shape
    k_loc = received.shape[2]
    n_lat, n_tm, _, variables, span, lat_count = received.shape
    cols = n_tm * span
    block = (n_lat, n_tm, 1, variables, span, lat_count)
    return pl.pallas_call(
        filter_kernel,
        grid=(k_loc,),
        in_specs=[
            pl.BlockSpec((1, rows, width), lambda k: (k + first, 0, 0)),
            pl.BlockSpec(block, lambda k: (0, 0, k, 0, 0, 0)),
            pl.BlockSpec((1, 1, rows), lambda k: (k + first, 0, 0)),
        ],
        out_specs=pl.BlockSpec(block, lambda k: (0, 0, k, 0, 0, 0)),
        out_shape=jax.ShapeDtypeStruct(received.shape, out_dtype),
        scratch_shapes=[pltpu.VMEM((cols, width), jnp.bfloat16), pltpu.VMEM((cols, width), out_dtype)],
    )(hough_table, received, mask)


def body_inner(fields, vmodes, owner_map, hough_table, keep_mask):
    n_lat = lax.axis_size("lat")
    n_tm = lax.axis_size("tm")
    orders = owner_map.shape[0]
    group_size = n_lat // orders
    variables, lev, lat_count, _, span = fields.shape
    kmodes = vmodes.shape[1]
    k_loc = kmodes // n_tm
    block = lat_count * span
    flat = fields.transpose(3, 0, 1, 4, 2).reshape(orders, variables, lev, block)
    dest_order = order_of_slot(owner_map)[jnp.arange(n_lat, dtype=jnp.int32) // group_size]
    picked = jnp.take(flat, dest_order, axis=0, mode="clip")
    vm = vmodes.reshape(lev, n_tm, k_loc)
    outgoing = jnp.einsum(
        "jvlx,lus->jusvx", picked, vm, preferred_element_type=jnp.float32
    ).astype(jnp.bfloat16)
    mask = keep_mask.astype(jnp.float32).reshape(k_loc, 1, -1)
    out_dtype = jnp.bfloat16 if group_size == 1 else jnp.float32
    bounds = sorted({0, (k_loc * 2) // 8, max(1, (k_loc * 5) // 8), k_loc})
    pieces = []
    for q in range(len(bounds) - 1):
        first, k_chunk = bounds[q], bounds[q + 1] - bounds[q]
        part = outgoing[:, :, first:first + k_chunk]
        part = part.reshape(n_lat * n_tm, k_chunk * variables, block)
        incoming = lax.all_to_all(part, AXES, 0, 0, tiled=True)
        incoming = incoming.reshape(n_lat, n_tm, k_chunk, variables, span, lat_count)
        synth = filter_rows(hough_table, incoming, mask, out_dtype, first)
        synth = synth.reshape(n_lat * n_tm, k_chunk * variables, block)
        back = lax.all_to_all(synth, AXES, 0, 0, tiled=True)
        back = back.reshape(orders, group_size, n_tm * k_chunk * variables, block)
        back = back.sum(axis=1) if group_size > 1 else back[:, 0]
        back = jnp.take(back, owner_map, axis=0, mode="clip")
        pieces.append(back.reshape(orders, n_tm, k_chunk, variables, span, lat_count))
    result = jnp.concatenate(pieces, axis=2) if len(pieces) > 1 else pieces[0]
    result = result.reshape(orders, kmodes, variables, span, lat_count)
    return result.transpose(1, 2, 4, 0, 3).astype(jnp.bfloat16)


def solution(mesh):
    in_specs = (P(None, None, "lat", None, "tm"), P(), P(), P("tm", "lat", None), P("tm", "lat"))
    out_specs = P(None, None, "lat", None, "tm")
    return jax.shard_map(body_inner, mesh=mesh, in_specs=in_specs, out_specs=out_specs, check_vma=False)
```
